512 devices in a mesh: men: 32 (over z_lo, y, core), women: 16 (over z_hi, x).
Axes of the slice: x: 4, y: 4, z: 16 (z_hi: 4, z_lo: 4; z = z_hi * 4 + z_lo), core: 2. Of those that a mesh axis runs over, the one named last changes fastest.
Arguments:
- men_embed: bfloat16 [65536, 128], P(('men', 'women')), may hold values from -4 to 4
- women_embed: bfloat16 [16384, 128], P(('women', 'men')), may hold values from -4 to 4
- men_count: int32 [65536], P('men'), may hold values from 1 to 297, as said below
- women_count: int32 [16384], P('women'), may hold values from 1 to 299
- women_root: float32 [16384], P('women'), may hold values from 0.5 to 6, as said below
- men_cotangent: float32 [65536], P('men'), may hold values from -300 to 300
- women_cotangent: float32 [16384], P('women'), may hold values from 24 to 864, as said below
Outputs:
- men_grad: float32 [65536, 128], P(('men', 'women'))
- women_grad: float32 [16384, 128], P(('women', 'men'))
The draws below stay inside these ranges and needn't reach their ends.
Inputs may be any that keep to these rules, and one draw needn't show every extreme that they name: `men_count`: integer masses of the male types. `women_root`: positive. `women_cotangent`: positive.
All inputs are finite; a program needn't handle non-finite values.
Results may differ from the reference program's by a relative error of at most 0.0031.
Values may be sent and summed in bfloat16 or wider, within the bound.
No kernel may reach another device: no remote copies, remote signals or barrier semaphores. Data moves between devices by JAX's collectives and lax.ppermute only.
A program may use at most 64 MiB of HBM per device.

```python
import math
import jax
import jax.numpy as jnp
from jax import lax

EMB = 128
MEN = 65536
WOMEN = 16384


def draw_men_count(key, part):
    base_mass = jax.random.randint(key, (MEN,), 1, 100, dtype=jnp.int32)
    levels = 1 + 3 * jnp.arange(MEN, dtype=jnp.int32) // MEN
    return (base_mass * levels).astype(jnp.int32)


def draw_women_root(key, part):
    position = jnp.arange(WOMEN, dtype=jnp.float32) / WOMEN
    rising = 1.0 + 2.0 * position
    base_root = jnp.exp(jax.random.uniform(key, (WOMEN,), jnp.float32, math.log(0.5), math.log(2.0)))
    return (base_root * rising).astype(jnp.float32)


def draw_women_cotangent(key, part):
    position = jnp.arange(WOMEN, dtype=jnp.float32) / WOMEN
    base_cot = jnp.exp(jax.random.uniform(key, (WOMEN,), jnp.float32, math.log(48.0), math.log(192.0)))
    rising = 1.0 + 2.0 * position
    return (base_cot * rising).astype(jnp.float32)


def with_ends(result, own_key, smallest, largest):
    longest = result.shape.index(max(result.shape))
    spots = []
    for shift in (0, 1):
        where = [jax.random.randint(jax.random.fold_in(own_key, axis), (), 0, length) for axis, length in enumerate(result.shape)]
        where[longest] = (where[longest] + shift) % result.shape[longest]
        spots.append(tuple(where))
    return result.at[spots[0]].set(smallest).at[spots[1]].set(largest)


def block_scale(key, dims, shards, least, largest):
    level, own = 1.0, jax.random.fold_in(key, 6)
    for axis_at, parts in shards:
        steps = jnp.exp(jax.random.uniform(jax.random.fold_in(own, axis_at), (parts,), jnp.float32, least / len(shards), largest / len(shards)))
        level = level * jnp.repeat(steps, dims[axis_at] // parts).reshape([-1 if axis == axis_at else 1 for axis in range(len(dims))])
    return level


def scatter_about(own_key, extent, scale, most, split=(), kind=jnp.bfloat16):
    gain = block_scale(own_key, extent, split, -0.22, 0.18) if split else 1.0
    values = jax.random.normal(own_key, extent, jnp.float32) * scale * gain
    return jnp.minimum(jnp.maximum(values, -most), most).astype(kind)


def setup_inputs(seed: int = 0) -> dict:
    seeds = jax.random.split(jax.random.key(seed), 8)
    men_embed = scatter_about(seeds[0], (MEN, EMB), (EMB ** -0.25), 4.0, ((0, 512),))
    women_embed = scatter_about(seeds[1], (WOMEN, EMB), (EMB ** -0.25), 4.0, ((0, 512),))
    men_count = draw_men_count(jax.random.fold_in(seeds[7], 71), 0)
    women_count = with_ends(jax.random.randint(seeds[3], (WOMEN,), 1, 300), jax.random.fold_in(seeds[3], 1), 1, 299).astype(jnp.int32)
    women_root = draw_women_root(jax.random.fold_in(seeds[7], 71), 0)
    men_cotangent = scatter_about(seeds[5], (MEN,), (200.0 * WOMEN / MEN), 300.0, ((0, 32),), jnp.float32)
    women_cotangent = draw_women_cotangent(jax.random.fold_in(seeds[7], 71), 0)
    return dict(men_embed=men_embed, women_embed=women_embed, men_count=men_count, women_count=women_count, women_root=women_root, men_cotangent=men_cotangent, women_cotangent=women_cotangent)


def kernel_rows(men_block, women_full):
    return jnp.exp(0.5 * jnp.dot(men_block, women_full.T, preferred_element_type=jnp.float32))

def round_half(values):
    return lax.optimization_barrier(values.astype(jnp.bfloat16)).astype(jnp.float32)

def reference(men_embed, women_embed, men_count, women_count, women_root, men_cotangent, women_cotangent):
    men_full = men_embed.astype(jnp.float32)
    women_full = women_embed.astype(jnp.float32)
    men_mass = men_count.astype(jnp.float32)
    women_mass = women_count.astype(jnp.float32)
    row_total = men_full.shape[0]
    block_rows = math.gcd(row_total, 2048)
    block_number = row_total // block_rows
    men_blocks = men_full.reshape(block_number, block_rows, EMB)
    mass_blocks = men_mass.reshape(block_number, block_rows)
    cot_blocks = men_cotangent.reshape(block_number, block_rows)

    def first_pass(column_total, pieces):
        men_block, mass_block = pieces
        kernel = kernel_rows(men_block, women_full)
        weighted = kernel * women_root[None, :]
        row_mass = lax.optimization_barrier(jnp.sum(weighted, axis=1))
        disc_rows = jnp.sqrt(row_mass * row_mass + 4.0 * mass_block)
        root_rows = 2.0 * mass_block / (row_mass + disc_rows)
        product = jnp.dot(round_half(weighted), women_full, preferred_element_type=jnp.float32)
        column_total = column_total + lax.optimization_barrier(jnp.sum(kernel * root_rows[:, None], axis=0))
        return (column_total, (root_rows, disc_rows, product))
    col_mass, (men_root, men_disc, weighted_v) = lax.scan(first_pass, jnp.zeros((women_full.shape[0],), jnp.float32), (men_blocks, mass_blocks))
    women_disc = jnp.sqrt(col_mass * col_mass + 4.0 * women_mass)
    col_grad = -women_cotangent / women_disc

    def second_pass(women_total, pieces):
        men_block, root_rows, disc_rows, product, cot_rows = pieces
        kernel = kernel_rows(men_block, women_full)
        weighted = kernel * col_grad[None, :]
        row_cot = lax.optimization_barrier(jnp.sum(weighted, axis=1))
        direct = jnp.dot(round_half(weighted), women_full, preferred_element_type=jnp.float32)
        row_grad = -(cot_rows + root_rows * row_cot) / disc_rows
        men_part = 0.5 * (row_grad[:, None] * product + root_rows[:, None] * direct)
        tangent = round_half(0.5 * kernel * (row_grad[:, None] * women_root[None, :] + root_rows[:, None] * col_grad[None, :]))
        women_total = women_total + jnp.dot(tangent.T, men_block, preferred_element_type=jnp.float32)
        return (women_total, men_part)
    women_grad, men_parts = lax.scan(second_pass, jnp.zeros((women_full.shape[0], EMB), jnp.float32), (men_blocks, men_root, men_disc, weighted_v, cot_blocks))
    return (men_parts.reshape(row_total, EMB), women_grad)
```

```python
import jax
import jax.numpy as jnp
from jax import lax
from jax.sharding import Mesh
from jax.sharding import PartitionSpec as P

MEN_AXES = ("zl", "y", "c")
WOMEN_AXES = ("zh", "x")
ALL_AXES = MEN_AXES + WOMEN_AXES


def kernel_tile(men_rows, women_block):
    surplus = lax.dot_general(
        men_rows, women_block, (((1,), (1,)), ((), ())), preferred_element_type=jnp.float32
    )
    return jnp.exp(0.5 * surplus)


def nested_psum(x, axes):
    for a in axes:
        x = lax.psum(x, a)
    return x


def nested_gather(x, axes):
    for a in reversed(axes):
        x = lax.all_gather(x, a, axis=0, tiled=True)
    return x


def halving_scatter(x, axes, sizes, order):
    rows = x.shape[0]
    block = rows
    for n in sizes:
        block //= n
    x = x.reshape(tuple(sizes) + (block,) + x.shape[1:])
    for a in order:
        d = axes.index(a)
        n = sizes[axes.index(a)]
        me = lax.axis_index(a)
        k = n // 2
        while k >= 1:
            width = x.shape[d] // 2
            bit = (me // k) % 2
            keep = lax.dynamic_slice_in_dim(x, bit * width, width, axis=d)
            send = lax.dynamic_slice_in_dim(x, (1 - bit) * width, width, axis=d)
            got = lax.ppermute(send, a, [(i, i ^ k) for i in range(n)])
            x = keep + got
            k //= 2
    return x.reshape((block,) + x.shape[len(sizes) + 1 :])


def make_body(men_sizes, women_sizes):
    def body(
        men_embed, women_embed, men_count, women_count, women_root, men_cotangent, women_cotangent
    ):
        men_rows = nested_gather(men_embed, WOMEN_AXES)
        women_rows = nested_gather(women_embed, MEN_AXES)
        men_mass = men_count.astype(jnp.float32)
        women_mass = women_count.astype(jnp.float32)
        kernel = kernel_tile(men_rows, women_rows)

        weighted = kernel * women_root[None, :]
        weighted_v = jnp.dot(
            weighted.astype(jnp.bfloat16), women_rows, preferred_element_type=jnp.float32
        )
        row_mass = nested_psum(jnp.sum(weighted, axis=1), ("x", "zh"))
        men_disc = jnp.sqrt(row_mass * row_mass + 4.0 * men_mass)
        men_root = 2.0 * men_mass / (row_mass + men_disc)

        col_partial = jnp.sum(kernel * men_root[:, None], axis=0)
        col_mass = nested_psum(col_partial, ("c", "y", "zl"))
        women_disc = jnp.sqrt(col_mass * col_mass + 4.0 * women_mass)
        col_grad = -women_cotangent / women_disc

        weighted = kernel * col_grad[None, :]
        direct_v = jnp.dot(
            weighted.astype(jnp.bfloat16), women_rows, preferred_element_type=jnp.float32
        )
        row_cot = nested_psum(jnp.sum(weighted, axis=1), ("x", "zh"))
        row_grad = -(men_cotangent + men_root * row_cot) / men_disc
        men_term = 0.5 * (row_grad[:, None] * weighted_v + men_root[:, None] * direct_v)

        tangent = (
            0.5
            * kernel
            * (row_grad[:, None] * women_root[None, :] + men_root[:, None] * col_grad[None, :])
        ).astype(jnp.bfloat16)
        women_terms = lax.dot_general(
            tangent, men_rows, (((0,), (0,)), ((), ())), preferred_element_type=jnp.float32
        )
        men_grad = halving_scatter(men_term, WOMEN_AXES, women_sizes, ("x", "zh"))
        women_grad = halving_scatter(women_terms, MEN_AXES, men_sizes, ("c", "y", "zl"))
        return (men_grad, women_grad)

    return body


def solution(mesh):
    men_n, women_n = mesh.shape["men"], mesh.shape["women"]
    women_sizes = (women_n // 4, 4)
    men_sizes = (men_n // 8, 4, 2)
    fine = Mesh(mesh.devices.reshape(men_sizes + women_sizes), ALL_AXES)
    return jax.shard_map(
        make_body(men_sizes, women_sizes),
        mesh=fine,
        in_specs=(
            P(ALL_AXES, None),
            P(WOMEN_AXES + MEN_AXES, None),
            P(MEN_AXES),
            P(WOMEN_AXES),
            P(WOMEN_AXES),
            P(MEN_AXES),
            P(WOMEN_AXES),
        ),
        out_specs=(P(ALL_AXES, None), P(WOMEN_AXES + MEN_AXES, None)),
        check_vma=False,
    )
```

```python
import jax
import jax.numpy as jnp
from jax import lax
from jax.sharding import Mesh
from jax.sharding import PartitionSpec as P

MEN_AXES = ("zl", "y", "c")
WOMEN_AXES = ("zh", "x")
ALL_AXES = MEN_AXES + WOMEN_AXES


def kernel_tile(men_rows, women_block):
    surplus = lax.dot_general(
        men_rows, women_block, (((1,), (1,)), ((), ())), preferred_element_type=jnp.float32
    )
    return jnp.exp(0.5 * surplus)


def nested_psum(x, axes):
    for a in axes:
        x = lax.psum(x, a)
    return x


def ordered_gather(x, axes, order):
    got = []
    for a in order:
        x = lax.all_gather(x, a, axis=0, tiled=False)
        got.insert(0, a)
    lead = len(axes)
    x = jnp.transpose(x, [got.index(a) for a in axes] + list(range(lead, x.ndim)))
    return x.reshape((-1,) + x.shape[lead + 1 :])


def halving_scatter(x, axes, sizes, order):
    rows = x.shape[0]
    block = rows
    for n in sizes:
        block //= n
    x = x.reshape(tuple(sizes) + (block,) + x.shape[1:])
    for a in order:
        d = axes.index(a)
        n = sizes[axes.index(a)]
        me = lax.axis_index(a)
        k = n // 2
        while k >= 1:
            width = x.shape[d] // 2
            bit = (me // k) % 2
            keep = lax.dynamic_slice_in_dim(x, bit * width, width, axis=d)
            send = lax.dynamic_slice_in_dim(x, (1 - bit) * width, width, axis=d)
            got = lax.ppermute(send, a, [(i, i ^ k) for i in range(n)])
            x = keep + got
            k //= 2
    return x.reshape((block,) + x.shape[len(sizes) + 1 :])


def make_body(men_sizes, women_sizes):
    def body(
        men_embed, women_embed, men_count, women_count, women_root, men_cotangent, women_cotangent
    ):
        men_rows = ordered_gather(men_embed, WOMEN_AXES, ("zh", "x"))
        women_rows = ordered_gather(women_embed, MEN_AXES, ("zl", "y", "c"))
        men_mass = men_count.astype(jnp.float32)
        women_mass = women_count.astype(jnp.float32)
        kernel = kernel_tile(men_rows, women_rows)

        weighted = kernel * women_root[None, :]
        weighted_v = jnp.dot(
            weighted.astype(jnp.bfloat16), women_rows, preferred_element_type=jnp.float32
        )
        row_mass = nested_psum(jnp.sum(weighted, axis=1), ("x", "zh"))
        men_disc = jnp.sqrt(row_mass * row_mass + 4.0 * men_mass)
        men_root = 2.0 * men_mass / (row_mass + men_disc)

        col_partial = jnp.sum(kernel * men_root[:, None], axis=0)
        col_mass = nested_psum(col_partial, ("c", "y", "zl"))
        women_disc = jnp.sqrt(col_mass * col_mass + 4.0 * women_mass)
        col_grad = -women_cotangent / women_disc

        weighted = kernel * col_grad[None, :]
        direct_v = jnp.dot(
            weighted.astype(jnp.bfloat16), women_rows, preferred_element_type=jnp.float32
        )
        row_cot = nested_psum(jnp.sum(weighted, axis=1), ("x", "zh"))
        row_grad = -(men_cotangent + men_root * row_cot) / men_disc
        men_term = 0.5 * (row_grad[:, None] * weighted_v + men_root[:, None] * direct_v)
        men_grad = halving_scatter(men_term, WOMEN_AXES, women_sizes, ("x", "zh"))

        tangent = (
            0.5
            * kernel
            * (row_grad[:, None] * women_root[None, :] + men_root[:, None] * col_grad[None, :])
        ).astype(jnp.bfloat16)
        women_terms = lax.dot_general(
            tangent, men_rows, (((0,), (0,)), ((), ())), preferred_element_type=jnp.float32
        )
        women_grad = halving_scatter(women_terms, MEN_AXES, men_sizes, ("c", "y", "zl"))
        return (men_grad, women_grad)

    return body


def solution(mesh):
    men_n, women_n = mesh.shape["men"], mesh.shape["women"]
    women_sizes = (women_n // 4, 4)
    men_sizes = (men_n // 8, 4, 2)
    fine = Mesh(mesh.devices.reshape(men_sizes + women_sizes), ALL_AXES)
    return jax.shard_map(
        make_body(men_sizes, women_sizes),
        mesh=fine,
        in_specs=(
            P(ALL_AXES, None),
            P(WOMEN_AXES + MEN_AXES, None),
            P(MEN_AXES),
            P(WOMEN_AXES),
            P(WOMEN_AXES),
            P(MEN_AXES),
            P(WOMEN_AXES),
        ),
        out_specs=(P(ALL_AXES, None), P(WOMEN_AXES + MEN_AXES, None)),
        check_vma=False,
    )
```

```python
import jax
import jax.numpy as jnp
from jax import lax
from jax.sharding import Mesh
from jax.sharding import PartitionSpec as P

MEN_AXES = ("zl", "y", "c")
WOMEN_AXES = ("zh", "x")
ALL_AXES = MEN_AXES + WOMEN_AXES


def kernel_tile(men_rows, women_block):
    surplus = lax.dot_general(
        men_rows, women_block, (((1,), (1,)), ((), ())), preferred_element_type=jnp.float32
    )
    return jnp.exp(0.5 * surplus)


def nested_psum(x, axes):
    for a in axes:
        x = lax.psum(x, a)
    return x


def ordered_gather(x, axes, order):
    got = []
    for a in order:
        x = lax.all_gather(x, a, axis=0, tiled=False)
        got.insert(0, a)
    lead = len(axes)
    x = jnp.transpose(x, [got.index(a) for a in axes] + list(range(lead, x.ndim)))
    return x.reshape((-1,) + x.shape[lead + 1 :])


def halving_scatter(x, axes, sizes, order):
    rows = x.shape[0]
    block = rows
    for n in sizes:
        block //= n
    x = x.reshape(tuple(sizes) + (block,) + x.shape[1:])
    for a in order:
        d = axes.index(a)
        n = sizes[axes.index(a)]
        me = lax.axis_index(a)
        k = n // 2
        while k >= 1:
            width = x.shape[d] // 2
            bit = (me // k) % 2
            keep = lax.dynamic_slice_in_dim(x, bit * width, width, axis=d)
            send = lax.dynamic_slice_in_dim(x, (1 - bit) * width, width, axis=d)
            got = lax.ppermute(send, a, [(i, i ^ k) for i in range(n)])
            x = keep + got
            k //= 2
    return x.reshape((block,) + x.shape[len(sizes) + 1 :])


def a2a_scatter(x, sizes, axes, order):
    dims = list(axes)
    for a in order:
        d = dims.index(a)
        x = jnp.sum(lax.all_to_all(x, a, d, 0, tiled=False), axis=0)
        dims.pop(d)
    return x


def make_body(men_sizes, women_sizes):
    def body(
        men_embed, women_embed, men_count, women_count, women_root, men_cotangent, women_cotangent
    ):
        men_rows = ordered_gather(men_embed, WOMEN_AXES, ("zh", "x"))
        women_rows = ordered_gather(women_embed, MEN_AXES, ("zl", "y", "c"))
        men_mass = men_count.astype(jnp.float32)
        women_mass = women_count.astype(jnp.float32)
        kernel = kernel_tile(men_rows, women_rows)

        weighted = kernel * women_root[None, :]
        weighted_v = jnp.dot(
            weighted.astype(jnp.bfloat16), women_rows, preferred_element_type=jnp.float32
        )
        row_mass = nested_psum(jnp.sum(weighted, axis=1), ("x", "zh"))
        men_disc = jnp.sqrt(row_mass * row_mass + 4.0 * men_mass)
        men_root = 2.0 * men_mass / (row_mass + men_disc)

        col_partial = jnp.sum(kernel * men_root[:, None], axis=0)
        col_mass = nested_psum(col_partial, ("c", "y", "zl"))
        women_disc = jnp.sqrt(col_mass * col_mass + 4.0 * women_mass)
        col_grad = -women_cotangent / women_disc

        weighted = kernel * col_grad[None, :]
        direct_v = jnp.dot(
            weighted.astype(jnp.bfloat16), women_rows, preferred_element_type=jnp.float32
        )
        row_cot = nested_psum(jnp.sum(weighted, axis=1), ("x", "zh"))
        row_grad = -(men_cotangent + men_root * row_cot) / men_disc
        men_term = 0.5 * (row_grad[:, None] * weighted_v + men_root[:, None] * direct_v)
        blk = men_term.shape[0] // (women_sizes[0] * women_sizes[1])
        part = a2a_scatter(
            men_term.reshape(women_sizes + (blk, men_term.shape[1])), women_sizes, WOMEN_AXES, ("x",)
        )
        men_grad = halving_scatter(
            part.reshape(-1, part.shape[-1]), ("zh",), (women_sizes[0],), ("zh",)
        )

        tangent = (
            0.5
            * kernel
            * (row_grad[:, None] * women_root[None, :] + men_root[:, None] * col_grad[None, :])
        ).astype(jnp.bfloat16)
        women_terms = lax.dot_general(
            tangent, men_rows, (((0,), (0,)), ((), ())), preferred_element_type=jnp.float32
        )
        blk = women_terms.shape[0] // (men_sizes[0] * men_sizes[1] * men_sizes[2])
        women_grad = a2a_scatter(
            women_terms.reshape(men_sizes + (blk, women_terms.shape[1])),
            men_sizes,
            MEN_AXES,
            ("c", "y", "zl"),
        )
        return (men_grad, women_grad)

    return body


def solution(mesh):
    men_n, women_n = mesh.shape["men"], mesh.shape["women"]
    women_sizes = (women_n // 4, 4)
    men_sizes = (men_n // 8, 4, 2)
    fine = Mesh(mesh.devices.reshape(men_sizes + women_sizes), ALL_AXES)
    return jax.shard_map(
        make_body(men_sizes, women_sizes),
        mesh=fine,
        in_specs=(
            P(ALL_AXES, None),
            P(WOMEN_AXES + MEN_AXES, None),
            P(MEN_AXES),
            P(WOMEN_AXES),
            P(WOMEN_AXES),
            P(MEN_AXES),
            P(WOMEN_AXES),
        ),
        out_specs=(P(ALL_AXES, None), P(WOMEN_AXES + MEN_AXES, None)),
        check_vma=False,
    )
```

```python
import jax
import jax.numpy as jnp
from jax import lax
from jax.sharding import Mesh
from jax.sharding import PartitionSpec as P

MEN_AXES = ("zl", "y", "c")
WOMEN_AXES = ("zh", "x")
ALL_AXES = MEN_AXES + WOMEN_AXES


def kernel_tile(men_rows, women_block):
    surplus = lax.dot_general(
        men_rows, women_block, (((1,), (1,)), ((), ())), preferred_element_type=jnp.float32
    )
    return jnp.exp(0.5 * surplus)


def nested_psum(x, axes):
    for a in axes:
        x = lax.psum(x, a)
    return x


def ordered_gather(x, axes, order):
    got = []
    for a in order:
        n = lax.axis_size(a)
        x = lax.all_to_all(jnp.broadcast_to(x[None], (n,) + x.shape), a, 0, 0, tiled=False)
        got.insert(0, a)
    lead = len(axes)
    x = jnp.transpose(x, [got.index(a) for a in axes] + list(range(lead, x.ndim)))
    return x.reshape((-1,) + x.shape[lead + 1 :])


def halving_scatter(x, axes, sizes, order):
    rows = x.shape[0]
    block = rows
    for n in sizes:
        block //= n
    x = x.reshape(tuple(sizes) + (block,) + x.shape[1:])
    for a in order:
        d = axes.index(a)
        n = sizes[axes.index(a)]
        me = lax.axis_index(a)
        k = n // 2
        while k >= 1:
            width = x.shape[d] // 2
            bit = (me // k) % 2
            keep = lax.dynamic_slice_in_dim(x, bit * width, width, axis=d)
            send = lax.dynamic_slice_in_dim(x, (1 - bit) * width, width, axis=d)
            got = lax.ppermute(send, a, [(i, i ^ k) for i in range(n)])
            x = keep + got
            k //= 2
    return x.reshape((block,) + x.shape[len(sizes) + 1 :])


def a2a_scatter(x, sizes, axes, order):
    dims = list(axes)
    for a in order:
        d = dims.index(a)
        x = jnp.sum(lax.all_to_all(x, a, d, 0, tiled=False), axis=0)
        dims.pop(d)
    return x


def make_body(men_sizes, women_sizes):
    def body(
        men_embed, women_embed, men_count, women_count, women_root, men_cotangent, women_cotangent
    ):
        men_rows = ordered_gather(men_embed, WOMEN_AXES, ("zh", "x"))
        women_rows = ordered_gather(women_embed, MEN_AXES, ("zl", "y", "c"))
        men_mass = men_count.astype(jnp.float32)
        women_mass = women_count.astype(jnp.float32)
        kernel = kernel_tile(men_rows, women_rows)

        weighted = kernel * women_root[None, :]
        weighted_v = jnp.dot(
            weighted.astype(jnp.bfloat16), women_rows, preferred_element_type=jnp.float32
        )
        row_mass = nested_psum(jnp.sum(weighted, axis=1), ("x", "zh"))
        men_disc = jnp.sqrt(row_mass * row_mass + 4.0 * men_mass)
        men_root = 2.0 * men_mass / (row_mass + men_disc)

        col_partial = jnp.sum(kernel * men_root[:, None], axis=0)
        col_mass = nested_psum(col_partial, ("c", "y", "zl"))
        women_disc = jnp.sqrt(col_mass * col_mass + 4.0 * women_mass)
        col_grad = -women_cotangent / women_disc

        weighted = kernel * col_grad[None, :]
        direct_v = jnp.dot(
            weighted.astype(jnp.bfloat16), women_rows, preferred_element_type=jnp.float32
        )
        row_cot = nested_psum(jnp.sum(weighted, axis=1), ("x", "zh"))
        row_grad = -(men_cotangent + men_root * row_cot) / men_disc
        men_term = 0.5 * (row_grad[:, None] * weighted_v + men_root[:, None] * direct_v)
        blk = men_term.shape[0] // (women_sizes[0] * women_sizes[1])
        part = a2a_scatter(
            men_term.reshape(women_sizes + (blk, men_term.shape[1])), women_sizes, WOMEN_AXES, ("x",)
        )
        men_grad = halving_scatter(
            part.reshape(-1, part.shape[-1]), ("zh",), (women_sizes[0],), ("zh",)
        )

        tangent = (
            0.5
            * kernel
            * (row_grad[:, None] * women_root[None, :] + men_root[:, None] * col_grad[None, :])
        ).astype(jnp.bfloat16)
        women_terms = lax.dot_general(
            tangent, men_rows, (((0,), (0,)), ((), ())), preferred_element_type=jnp.float32
        )
        blk = women_terms.shape[0] // (men_sizes[0] * men_sizes[1] * men_sizes[2])
        women_grad = a2a_scatter(
            women_terms.reshape(men_sizes + (blk, women_terms.shape[1])),
            men_sizes,
            MEN_AXES,
            ("c", "y", "zl"),
        )
        return (men_grad, women_grad)

    return body


def solution(mesh):
    men_n, women_n = mesh.shape["men"], mesh.shape["women"]
    women_sizes = (women_n // 4, 4)
    men_sizes = (men_n // 8, 4, 2)
    fine = Mesh(mesh.devices.reshape(men_sizes + women_sizes), ALL_AXES)
    return jax.shard_map(
        make_body(men_sizes, women_sizes),
        mesh=fine,
        in_specs=(
            P(ALL_AXES, None),
            P(WOMEN_AXES + MEN_AXES, None),
            P(MEN_AXES),
            P(WOMEN_AXES),
            P(WOMEN_AXES),
            P(MEN_AXES),
            P(WOMEN_AXES),
        ),
        out_specs=(P(ALL_AXES, None), P(WOMEN_AXES + MEN_AXES, None)),
        check_vma=False,
    )
```

```python
import jax
import jax.numpy as jnp
from jax import lax
from jax.sharding import Mesh
from jax.sharding import PartitionSpec as P

MEN_AXES = ("zl", "y", "c")
WOMEN_AXES = ("zh", "x")
ALL_AXES = MEN_AXES + WOMEN_AXES


def kernel_tile(men_rows, women_block):
    surplus = lax.dot_general(
        men_rows, women_block, (((1,), (1,)), ((), ())), preferred_element_type=jnp.float32
    )
    return jnp.exp(0.5 * surplus)


def nested_psum(x, axes):
    for a in axes:
        x = lax.psum(x, a)
    return x


def ordered_gather(x, axes, order):
    got = []
    for a in order:
        n = lax.axis_size(a)
        x = lax.all_to_all(jnp.broadcast_to(x[None], (n,) + x.shape), a, 0, 0, tiled=False)
        got.insert(0, a)
    lead = len(axes)
    x = jnp.transpose(x, [got.index(a) for a in axes] + list(range(lead, x.ndim)))
    return x.reshape((-1,) + x.shape[lead + 1 :])


def doubling_gather(x, axis, n):
    me = lax.axis_index(axis)
    x = x[None]
    k = 1
    while k < n:
        got = lax.ppermute(x, axis, [(i, i ^ k) for i in range(n)])
        low = (me // k) % 2 == 0
        x = jnp.concatenate([jnp.where(low, x, got), jnp.where(low, got, x)], axis=0)
        k *= 2
    return x


def halving_scatter(x, axes, sizes, order):
    rows = x.shape[0]
    block = rows
    for n in sizes:
        block //= n
    x = x.reshape(tuple(sizes) + (block,) + x.shape[1:])
    for a in order:
        d = axes.index(a)
        n = sizes[axes.index(a)]
        me = lax.axis_index(a)
        k = n // 2
        while k >= 1:
            width = x.shape[d] // 2
            bit = (me // k) % 2
            keep = lax.dynamic_slice_in_dim(x, bit * width, width, axis=d)
            send = lax.dynamic_slice_in_dim(x, (1 - bit) * width, width, axis=d)
            got = lax.ppermute(send, a, [(i, i ^ k) for i in range(n)])
            x = keep + got
            k //= 2
    return x.reshape((block,) + x.shape[len(sizes) + 1 :])


def a2a_scatter(x, sizes, axes, order):
    dims = list(axes)
    for a in order:
        d = dims.index(a)
        x = jnp.sum(lax.all_to_all(x, a, d, 0, tiled=False), axis=0)
        dims.pop(d)
    return x


def make_body(men_sizes, women_sizes):
    def body(
        men_embed, women_embed, men_count, women_count, women_root, men_cotangent, women_cotangent
    ):
        part = doubling_gather(men_embed, "zh", women_sizes[0])
        n = women_sizes[1]
        part = lax.all_to_all(jnp.broadcast_to(part[None], (n,) + part.shape), "x", 0, 0, tiled=False)
        men_rows = jnp.swapaxes(part, 0, 1).reshape((-1,) + men_embed.shape[1:])
        women_rows = ordered_gather(women_embed, MEN_AXES, ("zl", "y", "c"))
        men_mass = men_count.astype(jnp.float32)
        women_mass = women_count.astype(jnp.float32)
        kernel = kernel_tile(men_rows, women_rows)

        weighted = kernel * women_root[None, :]
        weighted_v = jnp.dot(
            weighted.astype(jnp.bfloat16), women_rows, preferred_element_type=jnp.float32
        )
        row_mass = nested_psum(jnp.sum(weighted, axis=1), ("x", "zh"))
        men_disc = jnp.sqrt(row_mass * row_mass + 4.0 * men_mass)
        men_root = 2.0 * men_mass / (row_mass + men_disc)

        col_partial = jnp.sum(kernel * men_root[:, None], axis=0)
        col_mass = nested_psum(col_partial, ("c", "y", "zl"))
        women_disc = jnp.sqrt(col_mass * col_mass + 4.0 * women_mass)
        col_grad = -women_cotangent / women_disc

        weighted = kernel * col_grad[None, :]
        direct_v = jnp.dot(
            weighted.astype(jnp.bfloat16), women_rows, preferred_element_type=jnp.float32
        )
        row_cot = nested_psum(jnp.sum(weighted, axis=1), ("x", "zh"))
        row_grad = -(men_cotangent + men_root * row_cot) / men_disc
        men_term = 0.5 * (row_grad[:, None] * weighted_v + men_root[:, None] * direct_v)
        blk = men_term.shape[0] // (women_sizes[0] * women_sizes[1])
        part = a2a_scatter(
            men_term.reshape(women_sizes + (blk, men_term.shape[1])), women_sizes, WOMEN_AXES, ("x",)
        )
        men_grad = halving_scatter(
            part.reshape(-1, part.shape[-1]), ("zh",), (women_sizes[0],), ("zh",)
        )

        tangent = (
            0.5
            * kernel
            * (row_grad[:, None] * women_root[None, :] + men_root[:, None] * col_grad[None, :])
        ).astype(jnp.bfloat16)
        women_terms = lax.dot_general(
            tangent, men_rows, (((0,), (0,)), ((), ())), preferred_element_type=jnp.float32
        )
        blk = women_terms.shape[0] // (men_sizes[0] * men_sizes[1] * men_sizes[2])
        women_grad = a2a_scatter(
            women_terms.reshape(men_sizes + (blk, women_terms.shape[1])),
            men_sizes,
            MEN_AXES,
            ("c", "y", "zl"),
        )
        return (men_grad, women_grad)

    return body


def solution(mesh):
    men_n, women_n = mesh.shape["men"], mesh.shape["women"]
    women_sizes = (women_n // 4, 4)
    men_sizes = (men_n // 8, 4, 2)
    fine = Mesh(mesh.devices.reshape(men_sizes + women_sizes), ALL_AXES)
    return jax.shard_map(
        make_body(men_sizes, women_sizes),
        mesh=fine,
        in_specs=(
            P(ALL_AXES, None),
            P(WOMEN_AXES + MEN_AXES, None),
            P(MEN_AXES),
            P(WOMEN_AXES),
            P(WOMEN_AXES),
            P(MEN_AXES),
            P(WOMEN_AXES),
        ),
        out_specs=(P(ALL_AXES, None), P(WOMEN_AXES + MEN_AXES, None)),
        check_vma=False,
    )
```

```python
import jax
import jax.numpy as jnp
from jax import lax
from jax.sharding import Mesh
from jax.sharding import PartitionSpec as P

MEN_AXES = ("zl", "y", "c")
WOMEN_AXES = ("zh", "x")
ALL_AXES = MEN_AXES + WOMEN_AXES


def kernel_tile(men_rows, women_block):
    surplus = lax.dot_general(
        men_rows, women_block, (((1,), (1,)), ((), ())), preferred_element_type=jnp.float32
    )
    return jnp.exp(0.5 * surplus)


def nested_psum(x, axes):
    for a in axes:
        x = lax.psum(x, a)
    return x


def ordered_gather(x, axes, order):
    got = []
    for a in order:
        n = lax.axis_size(a)
        x = lax.all_to_all(jnp.broadcast_to(x[None], (n,) + x.shape), a, 0, 0, tiled=False)
        got.insert(0, a)
    lead = len(axes)
    x = jnp.transpose(x, [got.index(a) for a in axes] + list(range(lead, x.ndim)))
    return x.reshape((-1,) + x.shape[lead + 1 :])


def halving_scatter(x, axes, sizes, order):
    rows = x.shape[0]
    block = rows
    for n in sizes:
        block //= n
    x = x.reshape(tuple(sizes) + (block,) + x.shape[1:])
    for a in order:
        d = axes.index(a)
        n = sizes[axes.index(a)]
        me = lax.axis_index(a)
        k = n // 2
        while k >= 1:
            width = x.shape[d] // 2
            bit = (me // k) % 2
            keep = lax.dynamic_slice_in_dim(x, bit * width, width, axis=d)
            send = lax.dynamic_slice_in_dim(x, (1 - bit) * width, width, axis=d)
            got = lax.ppermute(send, a, [(i, i ^ k) for i in range(n)])
            x = keep + got
            k //= 2
    return x.reshape((block,) + x.shape[len(sizes) + 1 :])


def a2a_scatter(x, sizes, axes, order):
    dims = list(axes)
    for a in order:
        d = dims.index(a)
        x = jnp.sum(lax.all_to_all(x, a, d, 0, tiled=False), axis=0)
        dims.pop(d)
    return x


def make_body(men_sizes, women_sizes):
    def body(
        men_embed, women_embed, men_count, women_count, women_root, men_cotangent, women_cotangent
    ):
        men_rows = ordered_gather(men_embed, WOMEN_AXES, ("zh", "x"))
        women_rows = ordered_gather(women_embed, MEN_AXES, ("zl", "y", "c"))
        men_mass = men_count.astype(jnp.float32)
        women_mass = women_count.astype(jnp.float32)
        kernel = kernel_tile(men_rows, women_rows)

        weighted = kernel * women_root[None, :]
        weighted_v = jnp.dot(
            weighted.astype(jnp.bfloat16), women_rows, preferred_element_type=jnp.float32
        )
        blk = weighted_v.shape[0] // (women_sizes[0] * women_sizes[1])
        wv_part = a2a_scatter(
            weighted_v.reshape(women_sizes + (blk, weighted_v.shape[1])), women_sizes, WOMEN_AXES, ("x",)
        )
        row_mass = nested_psum(jnp.sum(weighted, axis=1), ("x", "zh"))
        men_disc = jnp.sqrt(row_mass * row_mass + 4.0 * men_mass)
        men_root = 2.0 * men_mass / (row_mass + men_disc)

        col_partial = jnp.sum(kernel * men_root[:, None], axis=0)
        col_mass = nested_psum(col_partial, ("c", "y", "zl"))
        women_disc = jnp.sqrt(col_mass * col_mass + 4.0 * women_mass)
        col_grad = -women_cotangent / women_disc

        weighted = kernel * col_grad[None, :]
        direct_v = jnp.dot(
            weighted.astype(jnp.bfloat16), women_rows, preferred_element_type=jnp.float32
        )
        dv_part = a2a_scatter(
            direct_v.reshape(women_sizes + (blk, direct_v.shape[1])), women_sizes, WOMEN_AXES, ("x",)
        )
        row_cot = nested_psum(jnp.sum(weighted, axis=1), ("x", "zh"))
        row_grad = -(men_cotangent + men_root * row_cot) / men_disc
        both = jnp.stack([wv_part, dv_part], axis=1)
        both = halving_scatter(both.reshape(-1, both.shape[-1]), ("zh",), (women_sizes[0],), ("zh",))
        both = both.reshape(2, blk, both.shape[-1])
        start = (lax.axis_index("zh") * women_sizes[1] + lax.axis_index("x")) * blk
        grad_blk = lax.dynamic_slice_in_dim(row_grad, start, blk)
        root_blk = lax.dynamic_slice_in_dim(men_root, start, blk)
        men_grad = 0.5 * (grad_blk[:, None] * both[0] + root_blk[:, None] * both[1])

        tangent = (
            0.5
            * kernel
            * (row_grad[:, None] * women_root[None, :] + men_root[:, None] * col_grad[None, :])
        ).astype(jnp.bfloat16)
        women_terms = lax.dot_general(
            tangent, men_rows, (((0,), (0,)), ((), ())), preferred_element_type=jnp.float32
        )
        blk = women_terms.shape[0] // (men_sizes[0] * men_sizes[1] * men_sizes[2])
        women_grad = a2a_scatter(
            women_terms.reshape(men_sizes + (blk, women_terms.shape[1])),
            men_sizes,
            MEN_AXES,
            ("c", "y", "zl"),
        )
        return (men_grad, women_grad)

    return body


def solution(mesh):
    men_n, women_n = mesh.shape["men"], mesh.shape["women"]
    women_sizes = (women_n // 4, 4)
    men_sizes = (men_n // 8, 4, 2)
    fine = Mesh(mesh.devices.reshape(men_sizes + women_sizes), ALL_AXES)
    return jax.shard_map(
        make_body(men_sizes, women_sizes),
        mesh=fine,
        in_specs=(
            P(ALL_AXES, None),
            P(WOMEN_AXES + MEN_AXES, None),
            P(MEN_AXES),
            P(WOMEN_AXES),
            P(WOMEN_AXES),
            P(MEN_AXES),
            P(WOMEN_AXES),
        ),
        out_specs=(P(ALL_AXES, None), P(WOMEN_AXES + MEN_AXES, None)),
        check_vma=False,
    )
```

```python
import jax
import jax.numpy as jnp
from jax import lax
from jax.sharding import Mesh
from jax.sharding import PartitionSpec as P

MEN_AXES = ("zl", "y", "c")
WOMEN_AXES = ("zh", "x")
ALL_AXES = MEN_AXES + WOMEN_AXES


def kernel_tile(men_rows, women_block):
    surplus = lax.dot_general(
        men_rows, women_block, (((1,), (1,)), ((), ())), preferred_element_type=jnp.float32
    )
    return jnp.exp(0.5 * surplus)


def nested_psum(x, axes):
    for a in axes:
        x = lax.psum(x, a)
    return x


def ordered_gather(x, axes, order):
    got = []
    for a in order:
        n = lax.axis_size(a)
        x = lax.all_to_all(jnp.broadcast_to(x[None], (n,) + x.shape), a, 0, 0, tiled=False)
        got.insert(0, a)
    lead = len(axes)
    x = jnp.transpose(x, [got.index(a) for a in axes] + list(range(lead, x.ndim)))
    return x.reshape((-1,) + x.shape[lead + 1 :])


def halving_scatter(x, axes, sizes, order):
    rows = x.shape[0]
    block = rows
    for n in sizes:
        block //= n
    x = x.reshape(tuple(sizes) + (block,) + x.shape[1:])
    for a in order:
        d = axes.index(a)
        n = sizes[axes.index(a)]
        me = lax.axis_index(a)
        k = n // 2
        while k >= 1:
            width = x.shape[d] // 2
            bit = (me // k) % 2
            keep = lax.dynamic_slice_in_dim(x, bit * width, width, axis=d)
            send = lax.dynamic_slice_in_dim(x, (1 - bit) * width, width, axis=d)
            got = lax.ppermute(send, a, [(i, i ^ k) for i in range(n)])
            x = keep + got
            k //= 2
    return x.reshape((block,) + x.shape[len(sizes) + 1 :])


def a2a_scatter(x, sizes, axes, order):
    dims = list(axes)
    for a in order:
        d = dims.index(a)
        x = jnp.sum(lax.all_to_all(x, a, d, 0, tiled=False), axis=0)
        dims.pop(d)
    return x


def make_body(men_sizes, women_sizes):
    def body(
        men_embed, women_embed, men_count, women_count, women_root, men_cotangent, women_cotangent
    ):
        men_rows = ordered_gather(men_embed, WOMEN_AXES, ("zh", "x"))
        women_rows = ordered_gather(women_embed, MEN_AXES, ("zl", "y", "c"))
        men_mass = men_count.astype(jnp.float32)
        women_mass = women_count.astype(jnp.float32)
        kernel = kernel_tile(men_rows, women_rows)

        weighted = kernel * women_root[None, :]
        weighted_v = jnp.dot(
            weighted.astype(jnp.bfloat16), women_rows, preferred_element_type=jnp.float32
        )
        row_mass = nested_psum(jnp.sum(weighted, axis=1), ("x", "zh"))
        men_disc = jnp.sqrt(row_mass * row_mass + 4.0 * men_mass)
        men_root = 2.0 * men_mass / (row_mass + men_disc)

        col_partial = jnp.sum(kernel * men_root[:, None], axis=0)
        col_mass = nested_psum(col_partial, ("c", "y", "zl"))
        women_disc = jnp.sqrt(col_mass * col_mass + 4.0 * women_mass)
        col_grad = -women_cotangent / women_disc

        weighted = kernel * col_grad[None, :]
        direct_v = jnp.dot(
            weighted.astype(jnp.bfloat16), women_rows, preferred_element_type=jnp.float32
        )
        row_cot = nested_psum(jnp.sum(weighted, axis=1), ("x", "zh"))
        row_grad = -(men_cotangent + men_root * row_cot) / men_disc
        men_term = 0.5 * (row_grad[:, None] * weighted_v + men_root[:, None] * direct_v)
        blk = men_term.shape[0] // (women_sizes[0] * women_sizes[1])
        men_grad = a2a_scatter(
            men_term.reshape(women_sizes + (blk, men_term.shape[1])),
            women_sizes,
            WOMEN_AXES,
            ("x", "zh"),
        )

        tangent = (
            0.5
            * kernel
            * (row_grad[:, None] * women_root[None, :] + men_root[:, None] * col_grad[None, :])
        ).astype(jnp.bfloat16)
        women_terms = lax.dot_general(
            tangent, men_rows, (((0,), (0,)), ((), ())), preferred_element_type=jnp.float32
        )
        blk = women_terms.shape[0] // (men_sizes[0] * men_sizes[1] * men_sizes[2])
        women_grad = a2a_scatter(
            women_terms.reshape(men_sizes + (blk, women_terms.shape[1])),
            men_sizes,
            MEN_AXES,
            ("c", "y", "zl"),
        )
        return (men_grad, women_grad)

    return body


def solution(mesh):
    men_n, women_n = mesh.shape["men"], mesh.shape["women"]
    women_sizes = (women_n // 4, 4)
    men_sizes = (men_n // 8, 4, 2)
    fine = Mesh(mesh.devices.reshape(men_sizes + women_sizes), ALL_AXES)
    return jax.shard_map(
        make_body(men_sizes, women_sizes),
        mesh=fine,
        in_specs=(
            P(ALL_AXES, None),
            P(WOMEN_AXES + MEN_AXES, None),
            P(MEN_AXES),
            P(WOMEN_AXES),
            P(WOMEN_AXES),
            P(MEN_AXES),
            P(WOMEN_AXES),
        ),
        out_specs=(P(ALL_AXES, None), P(WOMEN_AXES + MEN_AXES, None)),
        check_vma=False,
    )
```

```python
import jax
import jax.numpy as jnp
from jax import lax
from jax.sharding import Mesh
from jax.sharding import PartitionSpec as P

MEN_AXES = ("zl", "y", "c")
WOMEN_AXES = ("zh", "x")
ALL_AXES = MEN_AXES + WOMEN_AXES


def kernel_tile(men_rows, women_block):
    surplus = lax.dot_general(
        men_rows, women_block, (((1,), (1,)), ((), ())), preferred_element_type=jnp.float32
    )
    return jnp.exp(0.5 * surplus)


def nested_psum(x, axes):
    for a in axes:
        x = lax.psum(x, a)
    return x


def ordered_gather(x, axes, order):
    got = []
    for a in order:
        if a == "zh":
            x = lax.all_gather(x, a, axis=0, tiled=False)
        else:
            n = lax.axis_size(a)
            x = lax.all_to_all(jnp.broadcast_to(x[None], (n,) + x.shape), a, 0, 0, tiled=False)
        got.insert(0, a)
    lead = len(axes)
    x = jnp.transpose(x, [got.index(a) for a in axes] + list(range(lead, x.ndim)))
    return x.reshape((-1,) + x.shape[lead + 1 :])


def halving_scatter(x, axes, sizes, order):
    rows = x.shape[0]
    block = rows
    for n in sizes:
        block //= n
    x = x.reshape(tuple(sizes) + (block,) + x.shape[1:])
    for a in order:
        d = axes.index(a)
        n = sizes[axes.index(a)]
        me = lax.axis_index(a)
        k = n // 2
        while k >= 1:
            width = x.shape[d] // 2
            bit = (me // k) % 2
            keep = lax.dynamic_slice_in_dim(x, bit * width, width, axis=d)
            send = lax.dynamic_slice_in_dim(x, (1 - bit) * width, width, axis=d)
            got = lax.ppermute(send, a, [(i, i ^ k) for i in range(n)])
            x = keep + got
            k //= 2
    return x.reshape((block,) + x.shape[len(sizes) + 1 :])


def a2a_scatter(x, sizes, axes, order):
    dims = list(axes)
    for a in order:
        d = dims.index(a)
        x = jnp.sum(lax.all_to_all(x, a, d, 0, tiled=False), axis=0)
        dims.pop(d)
    return x


def make_body(men_sizes, women_sizes):
    def body(
        men_embed, women_embed, men_count, women_count, women_root, men_cotangent, women_cotangent
    ):
        men_rows = ordered_gather(men_embed, WOMEN_AXES, ("zh", "x"))
        women_rows = ordered_gather(women_embed, MEN_AXES, ("zl", "y", "c"))
        men_mass = men_count.astype(jnp.float32)
        women_mass = women_count.astype(jnp.float32)
        kernel = kernel_tile(men_rows, women_rows)

        weighted = kernel * women_root[None, :]
        weighted_v = jnp.dot(
            weighted.astype(jnp.bfloat16), women_rows, preferred_element_type=jnp.float32
        )
        row_mass = nested_psum(jnp.sum(weighted, axis=1), ("x", "zh"))
        men_disc = jnp.sqrt(row_mass * row_mass + 4.0 * men_mass)
        men_root = 2.0 * men_mass / (row_mass + men_disc)

        col_partial = jnp.sum(kernel * men_root[:, None], axis=0)
        col_mass = nested_psum(col_partial, ("c", "y", "zl"))
        women_disc = jnp.sqrt(col_mass * col_mass + 4.0 * women_mass)
        col_grad = -women_cotangent / women_disc

        weighted = kernel * col_grad[None, :]
        direct_v = jnp.dot(
            weighted.astype(jnp.bfloat16), women_rows, preferred_element_type=jnp.float32
        )
        row_cot = nested_psum(jnp.sum(weighted, axis=1), ("x", "zh"))
        row_grad = -(men_cotangent + men_root * row_cot) / men_disc
        men_term = 0.5 * (row_grad[:, None] * weighted_v + men_root[:, None] * direct_v)
        blk = men_term.shape[0] // (women_sizes[0] * women_sizes[1])
        part = a2a_scatter(
            men_term.reshape(women_sizes + (blk, men_term.shape[1])), women_sizes, WOMEN_AXES, ("x",)
        )
        men_grad = halving_scatter(
            part.reshape(-1, part.shape[-1]), ("zh",), (women_sizes[0],), ("zh",)
        )

        tangent = (
            0.5
            * kernel
            * (row_grad[:, None] * women_root[None, :] + men_root[:, None] * col_grad[None, :])
        ).astype(jnp.bfloat16)
        women_terms = lax.dot_general(
            tangent, men_rows, (((0,), (0,)), ((), ())), preferred_element_type=jnp.float32
        )
        blk = women_terms.shape[0] // (men_sizes[0] * men_sizes[1] * men_sizes[2])
        women_grad = a2a_scatter(
            women_terms.reshape(men_sizes + (blk, women_terms.shape[1])),
            men_sizes,
            MEN_AXES,
            ("c", "y", "zl"),
        )
        return (men_grad, women_grad)

    return body


def solution(mesh):
    men_n, women_n = mesh.shape["men"], mesh.shape["women"]
    women_sizes = (women_n // 4, 4)
    men_sizes = (men_n // 8, 4, 2)
    fine = Mesh(mesh.devices.reshape(men_sizes + women_sizes), ALL_AXES)
    return jax.shard_map(
        make_body(men_sizes, women_sizes),
        mesh=fine,
        in_specs=(
            P(ALL_AXES, None),
            P(WOMEN_AXES + MEN_AXES, None),
            P(MEN_AXES),
            P(WOMEN_AXES),
            P(WOMEN_AXES),
            P(MEN_AXES),
            P(WOMEN_AXES),
        ),
        out_specs=(P(ALL_AXES, None), P(WOMEN_AXES + MEN_AXES, None)),
        check_vma=False,
    )
```

```python
import jax
import jax.numpy as jnp
from jax import lax
from jax.sharding import Mesh
from jax.sharding import PartitionSpec as P

MEN_AXES = ("zl", "y", "c")
WOMEN_AXES = ("zh", "x")
ALL_AXES = MEN_AXES + WOMEN_AXES


def kernel_tile(men_rows, women_block):
    surplus = lax.dot_general(
        men_rows, women_block, (((1,), (1,)), ((), ())), preferred_element_type=jnp.float32
    )
    return jnp.exp(0.5 * surplus)


def nested_psum(x, axes):
    for a in axes:
        x = lax.psum(x, a)
    return x


def ordered_gather(x, axes, order):
    got = []
    for a in order:
        if a in ("zh", "c"):
            x = lax.all_gather(x, a, axis=0, tiled=False)
        else:
            n = lax.axis_size(a)
            x = lax.all_to_all(jnp.broadcast_to(x[None], (n,) + x.shape), a, 0, 0, tiled=False)
        got.insert(0, a)
    lead = len(axes)
    x = jnp.transpose(x, [got.index(a) for a in axes] + list(range(lead, x.ndim)))
    return x.reshape((-1,) + x.shape[lead + 1 :])


def halving_scatter(x, axes, sizes, order):
    rows = x.shape[0]
    block = rows
    for n in sizes:
        block //= n
    x = x.reshape(tuple(sizes) + (block,) + x.shape[1:])
    for a in order:
        d = axes.index(a)
        n = sizes[axes.index(a)]
        me = lax.axis_index(a)
        k = n // 2
        while k >= 1:
            width = x.shape[d] // 2
            bit = (me // k) % 2
            keep = lax.dynamic_slice_in_dim(x, bit * width, width, axis=d)
            send = lax.dynamic_slice_in_dim(x, (1 - bit) * width, width, axis=d)
            got = lax.ppermute(send, a, [(i, i ^ k) for i in range(n)])
            x = keep + got
            k //= 2
    return x.reshape((block,) + x.shape[len(sizes) + 1 :])


def a2a_scatter(x, sizes, axes, order):
    dims = list(axes)
    for a in order:
        d = dims.index(a)
        x = jnp.sum(lax.all_to_all(x, a, d, 0, tiled=False), axis=0)
        dims.pop(d)
    return x


def make_body(men_sizes, women_sizes):
    def body(
        men_embed, women_embed, men_count, women_count, women_root, men_cotangent, women_cotangent
    ):
        men_rows = ordered_gather(men_embed, WOMEN_AXES, ("zh", "x"))
        women_rows = ordered_gather(women_embed, MEN_AXES, ("zl", "y", "c"))
        men_mass = men_count.astype(jnp.float32)
        women_mass = women_count.astype(jnp.float32)
        kernel = kernel_tile(men_rows, women_rows)

        weighted = kernel * women_root[None, :]
        weighted_v = jnp.dot(
            weighted.astype(jnp.bfloat16), women_rows, preferred_element_type=jnp.float32
        )
        row_mass = nested_psum(jnp.sum(weighted, axis=1), ("x", "zh"))
        men_disc = jnp.sqrt(row_mass * row_mass + 4.0 * men_mass)
        men_root = 2.0 * men_mass / (row_mass + men_disc)

        col_partial = jnp.sum(kernel * men_root[:, None], axis=0)
        col_mass = nested_psum(col_partial, ("c", "y", "zl"))
        women_disc = jnp.sqrt(col_mass * col_mass + 4.0 * women_mass)
        col_grad = -women_cotangent / women_disc

        weighted = kernel * col_grad[None, :]
        direct_v = jnp.dot(
            weighted.astype(jnp.bfloat16), women_rows, preferred_element_type=jnp.float32
        )
        row_cot = nested_psum(jnp.sum(weighted, axis=1), ("x", "zh"))
        row_grad = -(men_cotangent + men_root * row_cot) / men_disc
        men_term = 0.5 * (row_grad[:, None] * weighted_v + men_root[:, None] * direct_v)
        blk = men_term.shape[0] // (women_sizes[0] * women_sizes[1])
        part = a2a_scatter(
            men_term.reshape(women_sizes + (blk, men_term.shape[1])), women_sizes, WOMEN_AXES, ("x",)
        )
        men_grad = halving_scatter(
            part.reshape(-1, part.shape[-1]), ("zh",), (women_sizes[0],), ("zh",)
        )

        tangent = (
            0.5
            * kernel
            * (row_grad[:, None] * women_root[None, :] + men_root[:, None] * col_grad[None, :])
        ).astype(jnp.bfloat16)
        women_terms = lax.dot_general(
            tangent, men_rows, (((0,), (0,)), ((), ())), preferred_element_type=jnp.float32
        )
        blk = women_terms.shape[0] // (men_sizes[0] * men_sizes[1] * men_sizes[2])
        women_grad = a2a_scatter(
            women_terms.reshape(men_sizes + (blk, women_terms.shape[1])),
            men_sizes,
            MEN_AXES,
            ("c", "y", "zl"),
        )
        return (men_grad, women_grad)

    return body


def solution(mesh):
    men_n, women_n = mesh.shape["men"], mesh.shape["women"]
    women_sizes = (women_n // 4, 4)
    men_sizes = (men_n // 8, 4, 2)
    fine = Mesh(mesh.devices.reshape(men_sizes + women_sizes), ALL_AXES)
    return jax.shard_map(
        make_body(men_sizes, women_sizes),
        mesh=fine,
        in_specs=(
            P(ALL_AXES, None),
            P(WOMEN_AXES + MEN_AXES, None),
            P(MEN_AXES),
            P(WOMEN_AXES),
            P(WOMEN_AXES),
            P(MEN_AXES),
            P(WOMEN_AXES),
        ),
        out_specs=(P(ALL_AXES, None), P(WOMEN_AXES + MEN_AXES, None)),
        check_vma=False,
    )
```

```python
import jax
import jax.numpy as jnp
from jax import lax
from jax.sharding import Mesh
from jax.sharding import PartitionSpec as P

MEN_AXES = ("zl", "y", "c")
WOMEN_AXES = ("zh", "x")
ALL_AXES = MEN_AXES + WOMEN_AXES


def kernel_tile(men_rows, women_block):
    surplus = lax.dot_general(
        men_rows, women_block, (((1,), (1,)), ((), ())), preferred_element_type=jnp.float32
    )
    return jnp.exp(0.5 * surplus)


def nested_psum(x, axes):
    for a in axes:
        x = lax.psum(x, a)
    return x


def ordered_gather(x, axes, order):
    got = []
    for a in order:
        if a in ("zh", "c"):
            x = lax.all_gather(x, a, axis=0, tiled=False)
        else:
            n = lax.axis_size(a)
            x = lax.all_to_all(jnp.broadcast_to(x[None], (n,) + x.shape), a, 0, 0, tiled=False)
        got.insert(0, a)
    lead = len(axes)
    x = jnp.transpose(x, [got.index(a) for a in axes] + list(range(lead, x.ndim)))
    return x.reshape((-1,) + x.shape[lead + 1 :])


def halving_scatter(x, axes, sizes, order):
    rows = x.shape[0]
    block = rows
    for n in sizes:
        block //= n
    x = x.reshape(tuple(sizes) + (block,) + x.shape[1:])
    for a in order:
        d = axes.index(a)
        n = sizes[axes.index(a)]
        me = lax.axis_index(a)
        k = n // 2
        while k >= 1:
            width = x.shape[d] // 2
            bit = (me // k) % 2
            keep = lax.dynamic_slice_in_dim(x, bit * width, width, axis=d)
            send = lax.dynamic_slice_in_dim(x, (1 - bit) * width, width, axis=d)
            got = lax.ppermute(send, a, [(i, i ^ k) for i in range(n)])
            x = keep + got
            k //= 2
    return x.reshape((block,) + x.shape[len(sizes) + 1 :])


def a2a_scatter(x, sizes, axes, order):
    dims = list(axes)
    for a in order:
        d = dims.index(a)
        x = jnp.sum(lax.all_to_all(x, a, d, 0, tiled=False), axis=0)
        dims.pop(d)
    return x


def make_body(men_sizes, women_sizes):
    def body(
        men_embed, women_embed, men_count, women_count, women_root, men_cotangent, women_cotangent
    ):
        men_rows = ordered_gather(men_embed, WOMEN_AXES, ("zh", "x"))
        women_rows = ordered_gather(women_embed, MEN_AXES, ("zl", "y", "c"))
        men_mass = men_count.astype(jnp.float32)
        women_mass = women_count.astype(jnp.float32)
        kernel = kernel_tile(men_rows, women_rows)

        weighted = kernel * women_root[None, :]
        weighted_v = jnp.dot(
            weighted.astype(jnp.bfloat16), women_rows, preferred_element_type=jnp.float32
        )
        row_mass = nested_psum(jnp.sum(weighted, axis=1), ("x", "zh"))
        men_disc = jnp.sqrt(row_mass * row_mass + 4.0 * men_mass)
        men_root = 2.0 * men_mass / (row_mass + men_disc)

        col_partial = jnp.sum(kernel * men_root[:, None], axis=0)
        col_mass = nested_psum(col_partial, ("c", "y", "zl"))
        women_disc = jnp.sqrt(col_mass * col_mass + 4.0 * women_mass)
        col_grad = -women_cotangent / women_disc

        weighted = kernel * col_grad[None, :]
        direct_v = jnp.dot(
            weighted.astype(jnp.bfloat16), women_rows, preferred_element_type=jnp.float32
        )
        row_cot = nested_psum(jnp.sum(weighted, axis=1), ("x", "zh"))
        row_grad = -(men_cotangent + men_root * row_cot) / men_disc
        men_term = 0.5 * (row_grad[:, None] * weighted_v + men_root[:, None] * direct_v)
        blk = men_term.shape[0] // (women_sizes[0] * women_sizes[1])
        part = a2a_scatter(
            men_term.reshape(women_sizes + (blk, men_term.shape[1])), women_sizes, WOMEN_AXES, ("x",)
        )
        men_grad = halving_scatter(
            part.reshape(-1, part.shape[-1]), ("zh",), (women_sizes[0],), ("zh",)
        )

        tangent = (
            0.5
            * kernel
            * (row_grad[:, None] * women_root[None, :] + men_root[:, None] * col_grad[None, :])
        ).astype(jnp.bfloat16)
        women_terms = lax.dot_general(
            tangent, men_rows, (((0,), (0,)), ((), ())), preferred_element_type=jnp.float32
        )
        blk = women_terms.shape[0] // (men_sizes[0] * men_sizes[1] * men_sizes[2])
        part = women_terms.reshape(men_sizes + (blk, women_terms.shape[1]))
        bit = lax.axis_index("c")
        keep = lax.dynamic_index_in_dim(part, bit, axis=2, keepdims=False)
        send = lax.dynamic_index_in_dim(part, 1 - bit, axis=2, keepdims=False)
        part = keep + lax.ppermute(send, "c", [(0, 1), (1, 0)])
        women_grad = a2a_scatter(part, men_sizes[:2], MEN_AXES[:2], ("y", "zl"))
        return (men_grad, women_grad)

    return body


def solution(mesh):
    men_n, women_n = mesh.shape["men"], mesh.shape["women"]
    women_sizes = (women_n // 4, 4)
    men_sizes = (men_n // 8, 4, 2)
    fine = Mesh(mesh.devices.reshape(men_sizes + women_sizes), ALL_AXES)
    return jax.shard_map(
        make_body(men_sizes, women_sizes),
        mesh=fine,
        in_specs=(
            P(ALL_AXES, None),
            P(WOMEN_AXES + MEN_AXES, None),
            P(MEN_AXES),
            P(WOMEN_AXES),
            P(WOMEN_AXES),
            P(MEN_AXES),
            P(WOMEN_AXES),
        ),
        out_specs=(P(ALL_AXES, None), P(WOMEN_AXES + MEN_AXES, None)),
        check_vma=False,
    )
```
